768 devices in a mesh: dp: 16 (over x_hi, y), tile: 48 (over z, x_lo, core).
Axes of the slice: x: 4 (x_hi: 2, x_lo: 2; x = x_hi * 2 + x_lo), y: 8, z: 12, core: 2. Of those that a mesh axis runs over, the one named last changes fastest.
Arguments:
- section_map: bfloat16 [32, 192, 32, 3072], P('dp', 'tile'), may hold values from -16 to 16
- dw_kernel: bfloat16 [7, 7, 3072], replicated, may hold values from -0.875 to 0.875
- conv_bias: float32 [3072], replicated, may hold values from -3 to 3
- ln_gain: float32 [3072], replicated, may hold values from 0.5 to 1.5
- layer_scale: float32 [3072], replicated, may hold values from 0.25 to 1
- head_gain: float32 [3072], replicated, may hold values from 0.5 to 1.5
- head_weight: bfloat16 [3072, 1024], replicated, may hold values from -0.109375 to 0.109375
- texts: bfloat16 [192, 1024], P('dp'), may hold values from -6 to 6
- positives: int32 [192], replicated, may hold values from 0 to 191, each once
- sources: int32 [192], replicated, may hold values from 0 to 31
- numerators: int32 [32], replicated, may hold values from 1 to 8
Outputs:
- grad_map: bfloat16 [32, 192, 32, 3072], P('dp', 'tile')
- text_grad: float32 [192, 1024], P('dp')
- group_sums: float32 [32], replicated
The draws below stay inside these ranges and needn't reach their ends.
Inputs may be any that keep to these rules, and one draw needn't show every extreme that they name: `positives`: every text is the match of exactly one image.
All inputs are finite; a program needn't handle non-finite values.
Results may differ from the reference program's by a relative error of at most 0.0083.
Values may be sent and summed in bfloat16 or wider, within the bound.
No kernel may reach another device: no remote copies, remote signals or barrier semaphores. Data moves between devices by JAX's collectives and lax.ppermute only.
A program may use at most 64 MiB of HBM per device.

```python
import jax
import jax.numpy as jnp
from jax import lax

C = 3072
E = 1024
H = 32
W = 32
SOURCES = 32
ROWS = 192
BATCH = 32
NIMG = 192


def draw_section_map(key, part):
    row_place = (jnp.arange(ROWS) % H).astype(jnp.float32)
    rising = 1.0 + 2.0 * row_place / (H - 1)
    shape = (BATCH, ROWS, W, C)
    values = jax.random.normal(key, shape, jnp.float32) * rising[None, :, None, None]
    return jnp.clip(values, -16.0, 16.0).astype(jnp.bfloat16)


def touch_ends(entries, stream_key, smallest, top_value):
    spot = [jax.random.randint(jax.random.fold_in(stream_key, axis), (), 0, length) for axis, length in enumerate(entries.shape)]
    main_axis = entries.shape.index(max(entries.shape))
    next_to = spot[:main_axis] + [(spot[main_axis] + 1) % entries.shape[main_axis]] + spot[main_axis + 1:]
    return entries.at[tuple(spot)].set(smallest).at[tuple(next_to)].set(top_value)


def block_scale(key, dims, split, least, top_value):
    def one(axis_at, shards_of):
        heights = jax.random.uniform(jax.random.fold_in(jax.random.fold_in(key, 6), axis_at), (shards_of,), jnp.float32, least / len(split), top_value / len(split))
        return jnp.repeat(jnp.exp(heights), dims[axis_at] // shards_of).reshape((-1,) + (1,) * (len(dims) - axis_at - 1))

    level = one(*split[0])
    for cut in split[1:]:
        level = level * one(*cut)
    return level


def centred(stream_key, shape, width, bound, pieces=(), kind=jnp.bfloat16):
    values = jax.random.normal(stream_key, shape, jnp.float32) * width
    if len(pieces) > 0:
        values = block_scale(stream_key, shape, pieces, -0.22, 0.18) * values
    return jnp.clip(values, min=-bound, max=bound).astype(kind)


def setup_inputs(seed: int = 0) -> dict:
    keys = jax.random.split(jax.random.key(seed), 12)
    return {
        "section_map": draw_section_map(jax.random.fold_in(keys[11], 71), 0),
        "dw_kernel": centred(keys[1], (7, 7, C), 49 ** -0.5, 0.875),
        "conv_bias": centred(keys[2], (C,), 0.5, 3.0, (), jnp.float32),
        "ln_gain": jnp.clip(jax.random.uniform(keys[3], (C,), jnp.float32, 0.5, 1.5), 0.5, 1.5),
        "layer_scale": jnp.clip(jax.random.uniform(keys[4], (C,), jnp.float32, 0.25, 1.0), 0.25, 1.0),
        "head_gain": jnp.clip(jax.random.uniform(keys[5], (C,), jnp.float32, 0.5, 1.5), 0.5, 1.5),
        "head_weight": centred(keys[6], (C, E), C ** -0.5, 0.109375),
        "texts": centred(keys[7], (NIMG, E), 1.0, 6.0, ((0, 16),)),
        "positives": jax.random.permutation(keys[8], NIMG).astype(jnp.int32),
        "sources": touch_ends(jax.random.randint(keys[9], (NIMG,), 0, SOURCES), jax.random.fold_in(keys[9], 1), 0, SOURCES - 1).astype(jnp.int32),
        "numerators": touch_ends(jax.random.randint(keys[10], (SOURCES,), 1, 9), jax.random.fold_in(keys[10], 1), 1, 8).astype(jnp.int32),
    }


LOGIT_SCALE = 10.0
LOGIT_BIAS = -5.0

def cell_norm(values, gain):
    center = values - lax.optimization_barrier(jnp.mean(values, axis=-1, keepdims=True))
    spread = lax.optimization_barrier(jnp.mean(center * center, axis=-1, keepdims=True))
    return center * lax.rsqrt(spread + 1e-06) * gain

def unit_rows(values):
    return values * lax.rsqrt(lax.optimization_barrier(jnp.sum(values * values, axis=-1, keepdims=True)) + 1e-06)

def depthwise(image, kernel):
    padded = jnp.pad(image, ((3, 3), (3, 3), (0, 0)))
    summed = jnp.zeros((H, W, image.shape[-1]), jnp.float32)
    for tap_row in range(7):
        for tap_col in range(7):
            window = padded[tap_row:tap_row + H, tap_col:tap_col + W, :].astype(jnp.float32)
            summed = summed + window * kernel[tap_row, tap_col].astype(jnp.float32)
    return summed

def reference(section_map, dw_kernel, conv_bias, ln_gain, layer_scale, head_gain, head_weight, texts, positives, sources, numerators):
    images = section_map.reshape(NIMG, H, W, C)

    def forward_image(image):
        conved = depthwise(image, dw_kernel) + conv_bias
        section_out = image.astype(jnp.float32) + layer_scale * cell_norm(conved, ln_gain)
        return lax.optimization_barrier(jnp.sum(section_out, axis=(0, 1))) / (H * W)
    pooled = lax.map(forward_image, images)
    head_in = cell_norm(pooled, head_gain).astype(jnp.bfloat16)
    embed = jnp.dot(head_in, head_weight, preferred_element_type=jnp.float32)
    image_vec = unit_rows(embed).astype(jnp.bfloat16)
    text_f = texts.astype(jnp.float32)
    text_vec = unit_rows(text_f).astype(jnp.bfloat16)
    logits = LOGIT_SCALE * jnp.dot(image_vec, text_vec.T, preferred_element_type=jnp.float32) + LOGIT_BIAS
    labels = jnp.where(positives[:, None] == jnp.arange(NIMG, dtype=jnp.int32)[None, :], 1.0, -1.0).astype(jnp.float32)
    source_table = (sources[:, None] == jnp.arange(SOURCES, dtype=jnp.int32)[None, :]).astype(jnp.float32)
    weights = SOURCES * numerators[sources].astype(jnp.float32) / jnp.sum(numerators).astype(jnp.float32)
    row_loss = lax.optimization_barrier(jnp.sum(jax.nn.softplus(-labels * logits), axis=1))
    group_sums = lax.optimization_barrier(jnp.sum(source_table * (weights * row_loss)[:, None], axis=0))
    pair_grad = (weights[:, None] * -labels * jax.nn.sigmoid(-labels * logits)).astype(jnp.bfloat16)
    image_dir = LOGIT_SCALE * jnp.dot(pair_grad, text_vec, preferred_element_type=jnp.float32)
    text_dir = LOGIT_SCALE * jnp.dot(pair_grad.T, image_vec, preferred_element_type=jnp.float32)
    text_back = jax.vjp(unit_rows, text_f)[1]
    text_grad = text_back(text_dir)[0]
    embed_back = jax.vjp(unit_rows, embed)[1]
    embed_grad = embed_back(image_dir)[0].astype(jnp.bfloat16)
    head_grad = jnp.dot(embed_grad, head_weight.T, preferred_element_type=jnp.float32)
    pool_back = jax.vjp(lambda values: cell_norm(values, head_gain), pooled)[1]
    pooled_grad = pool_back(head_grad)[0]
    flipped = dw_kernel[::-1, ::-1, :]

    def backward_image(item):
        image, cotangent = item
        conved = depthwise(image, dw_kernel) + conv_bias
        norm_back = jax.vjp(lambda values: cell_norm(values, ln_gain), conved)[1]
        seeded = jnp.broadcast_to(layer_scale * cotangent, conved.shape)
        conv_grad = norm_back(seeded)[0].astype(jnp.bfloat16)
        spread = depthwise(conv_grad, flipped)
        return (cotangent + spread).astype(jnp.bfloat16)
    grad_images = lax.map(backward_image, (images, pooled_grad))
    grad_map = grad_images.reshape(section_map.shape)
    return (grad_map, text_grad, group_sums)
```

```python
import jax
import jax.numpy as jnp
from jax import lax
from jax.sharding import Mesh
from jax.sharding import PartitionSpec as P

H = 32
W = 32
SOURCES = 32


LOGIT_SCALE = 10.0
LOGIT_BIAS = -5.0


def halo_rows(value, width):
    devices = lax.axis_size("row")
    up = [(i, i + 1) for i in range(devices - 1)]
    down = [(j, i) for i, j in up]
    length = value.shape[1]
    last = lax.slice_in_dim(value, length - width, length, axis=1)
    leading = lax.slice_in_dim(value, 0, width, axis=1)
    before = lax.ppermute(last, "row", up)
    after = lax.ppermute(leading, "row", down)
    return jnp.concatenate([before, value, after], axis=1)


def group_sum(value):
    devices = lax.axis_size("row")
    step = 1
    while step < devices:
        pairs = [(i, i ^ step) for i in range(devices)]
        value = value + lax.ppermute(value, "row", pairs)
        step *= 2
    return value


def cell_norm(values, gain):
    center = values - jnp.mean(values, axis=-1, keepdims=True)
    spread = jnp.mean(center * center, axis=-1, keepdims=True)
    return center * lax.rsqrt(spread + 1e-06) * gain


def unit_rows(values):
    return values * lax.rsqrt(jnp.sum(values * values, axis=-1, keepdims=True) + 1e-06)


def depthwise_rows(field, kernel):
    batch_rows, row_count, width, channels = field.shape
    framed = halo_rows(field, 3)
    framed = jnp.pad(framed, ((0, 0), (0, 0), (3, 3), (0, 0)))
    summed = jnp.zeros(field.shape, jnp.float32)
    for tap_row in range(7):
        for tap_col in range(7):
            window = framed[:, tap_row : tap_row + row_count, tap_col : tap_col + width, :].astype(
                jnp.float32
            )
            summed = summed + window * kernel[tap_row, tap_col].astype(jnp.float32)
    return summed


def local(
    section_map,
    dw_kernel,
    conv_bias,
    ln_gain,
    layer_scale,
    head_gain,
    head_weight,
    texts,
    positives,
    sources,
    numerators,
):
    batch_rows, row_count, width, channels = section_map.shape
    img_count = lax.axis_size("img")
    dp_count = lax.axis_size("dp")
    dp_at = lax.axis_index("dp")
    img_at = lax.axis_index("img")
    conved = depthwise_rows(section_map, dw_kernel) + conv_bias
    section_out = section_map.astype(jnp.float32) + layer_scale * cell_norm(conved, ln_gain)
    partial_value = jnp.sum(section_out, axis=(1, 2)) / (H * W)
    pooled = group_sum(partial_value)
    head_in = cell_norm(pooled, head_gain).astype(jnp.bfloat16)
    embed = jnp.dot(head_in, head_weight, preferred_element_type=jnp.float32)
    image_vec = unit_rows(embed).astype(jnp.bfloat16)
    text_f = texts.astype(jnp.float32)
    text_vec = unit_rows(text_f).astype(jnp.bfloat16)
    text_count = texts.shape[0]
    share = text_count // img_count
    text_share = lax.dynamic_slice_in_dim(text_vec, img_at * share, share)
    payload = jnp.concatenate([image_vec, text_share], axis=0)
    gathered = lax.all_gather(payload, "img", axis=0)
    gathered = lax.all_gather(gathered, "dp", axis=0)
    image_all = jnp.transpose(gathered[:, :, :batch_rows, :], (0, 2, 1, 3)).reshape(
        dp_count * batch_rows * img_count, -1
    )
    text_all = gathered[:, :, batch_rows:, :].reshape(dp_count * text_count, -1)
    count = text_all.shape[0]
    logits = (
        LOGIT_SCALE * jnp.dot(image_all, text_all.T, preferred_element_type=jnp.float32)
        + LOGIT_BIAS
    )
    labels = jnp.where(positives[:, None] == jnp.arange(count)[None, :], 1.0, -1.0).astype(
        jnp.float32
    )
    source_table = (sources[:, None] == jnp.arange(SOURCES)[None, :]).astype(jnp.float32)
    weights = (
        SOURCES
        * numerators[sources].astype(jnp.float32)
        / jnp.sum(numerators).astype(jnp.float32)
    )
    row_loss = jnp.sum(jax.nn.softplus(-labels * logits), axis=1)
    group_sums = jnp.sum(source_table * (weights * row_loss)[:, None], axis=0)
    pair_grad = (weights[:, None] * -labels * jax.nn.sigmoid(-labels * logits)).astype(
        jnp.bfloat16
    )
    own_rows = (dp_at * batch_rows + jnp.arange(batch_rows)) * img_count + img_at
    own_pair = jnp.take(pair_grad, own_rows, axis=0)
    image_dir = LOGIT_SCALE * jnp.dot(own_pair, text_all, preferred_element_type=jnp.float32)
    text_pair = lax.dynamic_slice_in_dim(pair_grad, dp_at * text_count, text_count, axis=1)
    text_dir = LOGIT_SCALE * lax.dot_general(
        text_pair, image_all, (((0,), (0,)), ((), ())), preferred_element_type=jnp.float32
    )
    text_back = jax.vjp(unit_rows, text_f)[1]
    text_grad = text_back(text_dir)[0]
    embed_back = jax.vjp(unit_rows, embed)[1]
    embed_grad = embed_back(image_dir)[0].astype(jnp.bfloat16)
    head_grad = jnp.dot(embed_grad, head_weight.T, preferred_element_type=jnp.float32)
    pool_back = jax.vjp(lambda values: cell_norm(values, head_gain), pooled)[1]
    own_grad = pool_back(head_grad)[0]
    norm_back = jax.vjp(lambda values: cell_norm(values, ln_gain), conved)[1]
    seeded = jnp.broadcast_to((layer_scale * own_grad)[:, None, None, :], conved.shape)
    conv_grad = norm_back(seeded)[0].astype(jnp.bfloat16)
    spread = depthwise_rows(conv_grad, dw_kernel[::-1, ::-1, :])
    grad_map = (own_grad[:, None, None, :] + spread).astype(jnp.bfloat16)
    return (grad_map, text_grad, group_sums)


def solution(mesh):
    dp_count, tile_count = mesh.devices.shape

    def run(section_map, *rest):
        rows_each = section_map.shape[1] // tile_count
        per_image = H // rows_each
        assert per_image & (per_image - 1) == 0
        split = Mesh(
            mesh.devices.reshape(dp_count, tile_count // per_image, per_image),
            ("dp", "img", "row"),
        )
        tiled = ("img", "row")
        placed = (
            P("dp", tiled, None, None),
            P(),
            P(),
            P(),
            P(),
            P(),
            P(),
            P("dp", None),
            P(),
            P(),
            P(),
        )
        return jax.shard_map(
            local,
            mesh=split,
            in_specs=placed,
            out_specs=(P("dp", tiled, None, None), P("dp", None), P()),
            check_vma=False,
        )(section_map, *rest)

    return run
```

```python
import jax
import jax.numpy as jnp
from jax import lax
from jax.sharding import Mesh
from jax.sharding import PartitionSpec as P

H = 32
W = 32
SOURCES = 32


LOGIT_SCALE = 10.0
LOGIT_BIAS = -5.0


def halo_rows(value, width):
    devices = lax.axis_size("row")
    up = [(i, i + 1) for i in range(devices - 1)]
    down = [(j, i) for i, j in up]
    length = value.shape[1]
    last = lax.slice_in_dim(value, length - width, length, axis=1)
    leading = lax.slice_in_dim(value, 0, width, axis=1)
    before = lax.ppermute(last, "row", up)
    after = lax.ppermute(leading, "row", down)
    return jnp.concatenate([before, value, after], axis=1)


def group_sum(value):
    devices = lax.axis_size("row")
    step = 1
    while step < devices:
        pairs = [(i, i ^ step) for i in range(devices)]
        value = value + lax.ppermute(value, "row", pairs)
        step *= 2
    return value


def gather_stages(value, axis, radices):
    place = 1
    devices = lax.axis_size(axis)
    at = lax.axis_index(axis)
    for radix in radices:
        digit = (at // place) % radix
        got = [value]
        for shift in range(1, radix):
            pairs = []
            for src in range(devices):
                d = (src // place) % radix
                pairs.append((src, src + ((d + shift) % radix - d) * place))
            got.append(lax.ppermute(value, axis, pairs))
        stacked = jnp.stack(got)
        order = (digit - jnp.arange(radix)) % radix
        value = jnp.take(stacked, order, axis=0)
        place *= radix
    return value.reshape((devices,) + value.shape[len(radices) :])


def radix_split(count):
    parts = []
    for radix in (4, 3, 2):
        while count % radix == 0 and count > 1:
            parts.append(radix)
            count //= radix
    assert count == 1
    return parts


def cell_norm(values, gain):
    center = values - jnp.mean(values, axis=-1, keepdims=True)
    spread = jnp.mean(center * center, axis=-1, keepdims=True)
    return center * lax.rsqrt(spread + 1e-06) * gain


def unit_rows(values):
    return values * lax.rsqrt(jnp.sum(values * values, axis=-1, keepdims=True) + 1e-06)


def depthwise_rows(field, kernel):
    batch_rows, row_count, width, channels = field.shape
    framed = halo_rows(field, 3)
    framed = jnp.pad(framed, ((0, 0), (0, 0), (3, 3), (0, 0)))
    summed = jnp.zeros(field.shape, jnp.float32)
    for tap_row in range(7):
        for tap_col in range(7):
            window = framed[:, tap_row : tap_row + row_count, tap_col : tap_col + width, :].astype(
                jnp.float32
            )
            summed = summed + window * kernel[tap_row, tap_col].astype(jnp.float32)
    return summed


def local(
    section_map,
    dw_kernel,
    conv_bias,
    ln_gain,
    layer_scale,
    head_gain,
    head_weight,
    texts,
    positives,
    sources,
    numerators,
):
    batch_rows, row_count, width, channels = section_map.shape
    img_count = lax.axis_size("img")
    dp_count = lax.axis_size("dp")
    dp_at = lax.axis_index("dp")
    img_at = lax.axis_index("img")
    conved = depthwise_rows(section_map, dw_kernel) + conv_bias
    section_out = section_map.astype(jnp.float32) + layer_scale * cell_norm(conved, ln_gain)
    partial_value = jnp.sum(section_out, axis=(1, 2)) / (H * W)
    pooled = group_sum(partial_value)
    head_in = cell_norm(pooled, head_gain).astype(jnp.bfloat16)
    embed = jnp.dot(head_in, head_weight, preferred_element_type=jnp.float32)
    image_vec = unit_rows(embed).astype(jnp.bfloat16)
    text_f = texts.astype(jnp.float32)
    text_vec = unit_rows(text_f).astype(jnp.bfloat16)
    text_count = texts.shape[0]
    share = text_count // img_count
    text_share = lax.dynamic_slice_in_dim(text_vec, img_at * share, share)
    payload = jnp.concatenate([image_vec, text_share], axis=0)
    gathered = gather_stages(payload, "img", radix_split(img_count))
    gathered = gather_stages(gathered, "dp", radix_split(dp_count))
    image_all = jnp.transpose(gathered[:, :, :batch_rows, :], (0, 2, 1, 3)).reshape(
        dp_count * batch_rows * img_count, -1
    )
    text_all = gathered[:, :, batch_rows:, :].reshape(dp_count * text_count, -1)
    count = text_all.shape[0]
    logits = (
        LOGIT_SCALE * jnp.dot(image_all, text_all.T, preferred_element_type=jnp.float32)
        + LOGIT_BIAS
    )
    labels = jnp.where(positives[:, None] == jnp.arange(count)[None, :], 1.0, -1.0).astype(
        jnp.float32
    )
    source_table = (sources[:, None] == jnp.arange(SOURCES)[None, :]).astype(jnp.float32)
    weights = (
        SOURCES
        * numerators[sources].astype(jnp.float32)
        / jnp.sum(numerators).astype(jnp.float32)
    )
    row_loss = lax.optimization_barrier(jnp.sum(jax.nn.softplus(-labels * logits), axis=1))
    group_sums = jnp.sum(source_table * (weights * row_loss)[:, None], axis=0)
    pair_grad = (weights[:, None] * -labels * jax.nn.sigmoid(-labels * logits)).astype(
        jnp.bfloat16
    )
    own_rows = (dp_at * batch_rows + jnp.arange(batch_rows)) * img_count + img_at
    own_pair = jnp.take(pair_grad, own_rows, axis=0)
    image_dir = LOGIT_SCALE * jnp.dot(own_pair, text_all, preferred_element_type=jnp.float32)
    text_pair = lax.dynamic_slice_in_dim(pair_grad, dp_at * text_count, text_count, axis=1)
    text_dir = LOGIT_SCALE * lax.dot_general(
        text_pair, image_all, (((0,), (0,)), ((), ())), preferred_element_type=jnp.float32
    )
    text_back = jax.vjp(unit_rows, text_f)[1]
    text_grad = text_back(text_dir)[0]
    embed_back = jax.vjp(unit_rows, embed)[1]
    embed_grad = embed_back(image_dir)[0].astype(jnp.bfloat16)
    head_grad = jnp.dot(embed_grad, head_weight.T, preferred_element_type=jnp.float32)
    pool_back = jax.vjp(lambda values: cell_norm(values, head_gain), pooled)[1]
    own_grad = pool_back(head_grad)[0]
    norm_back = jax.vjp(lambda values: cell_norm(values, ln_gain), conved)[1]
    seeded = jnp.broadcast_to((layer_scale * own_grad)[:, None, None, :], conved.shape)
    conv_grad = norm_back(seeded)[0].astype(jnp.bfloat16)
    spread = depthwise_rows(conv_grad, dw_kernel[::-1, ::-1, :])
    grad_map = (own_grad[:, None, None, :] + spread).astype(jnp.bfloat16)
    return (grad_map, text_grad, group_sums)


def solution(mesh):
    dp_count, tile_count = mesh.devices.shape

    def run(section_map, *rest):
        rows_each = section_map.shape[1] // tile_count
        per_image = H // rows_each
        assert per_image & (per_image - 1) == 0
        split = Mesh(
            mesh.devices.reshape(dp_count, tile_count // per_image, per_image),
            ("dp", "img", "row"),
        )
        tiled = ("img", "row")
        placed = (
            P("dp", tiled, None, None),
            P(),
            P(),
            P(),
            P(),
            P(),
            P(),
            P("dp", None),
            P(),
            P(),
            P(),
        )
        return jax.shard_map(
            local,
            mesh=split,
            in_specs=placed,
            out_specs=(P("dp", tiled, None, None), P("dp", None), P()),
            check_vma=False,
        )(section_map, *rest)

    return run
```

```python
import jax
import jax.numpy as jnp
from jax import lax
from jax.sharding import Mesh
from jax.sharding import PartitionSpec as P

H = 32
W = 32
SOURCES = 32


LOGIT_SCALE = 10.0
LOGIT_BIAS = -5.0


def halo_rows(value, width):
    devices = lax.axis_size("row")
    up = [(i, i + 1) for i in range(devices - 1)]
    down = [(j, i) for i, j in up]
    length = value.shape[1]
    last = lax.slice_in_dim(value, length - width, length, axis=1)
    leading = lax.slice_in_dim(value, 0, width, axis=1)
    before = lax.ppermute(last, "row", up)
    after = lax.ppermute(leading, "row", down)
    return jnp.concatenate([before, value, after], axis=1)


def group_sum(value):
    devices = lax.axis_size("row")
    step = 1
    while step < devices:
        pairs = [(i, i ^ step) for i in range(devices)]
        value = value + lax.ppermute(value, "row", pairs)
        step *= 2
    return value


def gather_stages(value, axis, radices):
    place = 1
    devices = lax.axis_size(axis)
    at = lax.axis_index(axis)
    for radix in radices:
        digit = (at // place) % radix
        got = [value]
        for shift in range(1, radix):
            pairs = []
            for src in range(devices):
                d = (src // place) % radix
                pairs.append((src, src + ((d + shift) % radix - d) * place))
            got.append(lax.ppermute(value, axis, pairs))
        stacked = jnp.stack(got)
        order = (digit - jnp.arange(radix)) % radix
        value = jnp.take(stacked, order, axis=0)
        place *= radix
    return value.reshape((devices,) + value.shape[len(radices) :])


def radix_split(count):
    parts = []
    for radix in (3, 2):
        while count % radix == 0 and count > 1:
            parts.append(radix)
            count //= radix
    assert count == 1
    return parts


def cell_norm(values, gain):
    center = values - jnp.mean(values, axis=-1, keepdims=True)
    spread = jnp.mean(center * center, axis=-1, keepdims=True)
    return center * lax.rsqrt(spread + 1e-06) * gain


def unit_rows(values):
    return values * lax.rsqrt(jnp.sum(values * values, axis=-1, keepdims=True) + 1e-06)


def depthwise_rows(field, kernel):
    batch_rows, row_count, width, channels = field.shape
    framed = halo_rows(field, 3)
    framed = jnp.pad(framed, ((0, 0), (0, 0), (3, 3), (0, 0)))
    summed = jnp.zeros(field.shape, jnp.float32)
    for tap_row in range(7):
        for tap_col in range(7):
            window = framed[:, tap_row : tap_row + row_count, tap_col : tap_col + width, :].astype(
                jnp.float32
            )
            summed = summed + window * kernel[tap_row, tap_col].astype(jnp.float32)
    return summed


def local(
    section_map,
    dw_kernel,
    conv_bias,
    ln_gain,
    layer_scale,
    head_gain,
    head_weight,
    texts,
    positives,
    sources,
    numerators,
):
    batch_rows, row_count, width, channels = section_map.shape
    img_count = lax.axis_size("img")
    dp_count = lax.axis_size("dp")
    dp_at = lax.axis_index("dp")
    img_at = lax.axis_index("img")
    conved = depthwise_rows(section_map, dw_kernel) + conv_bias
    section_out = section_map.astype(jnp.float32) + layer_scale * cell_norm(conved, ln_gain)
    partial_value = jnp.sum(section_out, axis=(1, 2)) / (H * W)
    pooled = group_sum(partial_value)
    head_in = cell_norm(pooled, head_gain).astype(jnp.bfloat16)
    embed = jnp.dot(head_in, head_weight, preferred_element_type=jnp.float32)
    image_vec = unit_rows(embed).astype(jnp.bfloat16)
    text_f = texts.astype(jnp.float32)
    text_vec = unit_rows(text_f).astype(jnp.bfloat16)
    text_count = texts.shape[0]
    text_all = gather_stages(text_vec, "dp", radix_split(dp_count)).reshape(
        dp_count * text_count, -1
    )
    count = text_all.shape[0]
    source_table = (sources[:, None] == jnp.arange(SOURCES)[None, :]).astype(jnp.float32)
    weights = (
        SOURCES
        * jnp.sum(source_table * numerators.astype(jnp.float32)[None, :], axis=1)
        / jnp.sum(numerators).astype(jnp.float32)
    )
    own_rows = (dp_at * batch_rows + jnp.arange(batch_rows)) * img_count + img_at
    own_logits = (
        LOGIT_SCALE * jnp.dot(image_vec, text_all.T, preferred_element_type=jnp.float32)
        + LOGIT_BIAS
    )
    own_labels = jnp.where(
        jnp.take(positives, own_rows)[:, None] == jnp.arange(count)[None, :], 1.0, -1.0
    ).astype(jnp.float32)
    own_weights = jnp.take(weights, own_rows)
    own_pair = (
        own_weights[:, None] * -own_labels * jax.nn.sigmoid(-own_labels * own_logits)
    ).astype(jnp.bfloat16)
    image_dir = LOGIT_SCALE * jnp.dot(own_pair, text_all, preferred_element_type=jnp.float32)
    gathered = gather_stages(image_vec, "img", radix_split(img_count))
    gathered = gather_stages(gathered, "dp", radix_split(dp_count))
    image_all = jnp.transpose(gathered, (0, 2, 1, 3)).reshape(
        dp_count * batch_rows * img_count, -1
    )
    logits = (
        LOGIT_SCALE * jnp.dot(image_all, text_all.T, preferred_element_type=jnp.float32)
        + LOGIT_BIAS
    )
    labels = jnp.where(positives[:, None] == jnp.arange(count)[None, :], 1.0, -1.0).astype(
        jnp.float32
    )
    row_loss = lax.optimization_barrier(jnp.sum(jax.nn.softplus(-labels * logits), axis=1))
    group_sums = jnp.sum(source_table * (weights * row_loss)[:, None], axis=0)
    pair_grad = (weights[:, None] * -labels * jax.nn.sigmoid(-labels * logits)).astype(
        jnp.bfloat16
    )
    text_pair = lax.dynamic_slice_in_dim(pair_grad, dp_at * text_count, text_count, axis=1)
    text_dir = LOGIT_SCALE * lax.dot_general(
        text_pair, image_all, (((0,), (0,)), ((), ())), preferred_element_type=jnp.float32
    )
    text_back = jax.vjp(unit_rows, text_f)[1]
    text_grad = text_back(text_dir)[0]
    embed_back = jax.vjp(unit_rows, embed)[1]
    embed_grad = embed_back(image_dir)[0].astype(jnp.bfloat16)
    head_grad = jnp.dot(embed_grad, head_weight.T, preferred_element_type=jnp.float32)
    pool_back = jax.vjp(lambda values: cell_norm(values, head_gain), pooled)[1]
    own_grad = pool_back(head_grad)[0]
    norm_back = jax.vjp(lambda values: cell_norm(values, ln_gain), conved)[1]
    seeded = jnp.broadcast_to((layer_scale * own_grad)[:, None, None, :], conved.shape)
    conv_grad = norm_back(seeded)[0].astype(jnp.bfloat16)
    spread = depthwise_rows(conv_grad, dw_kernel[::-1, ::-1, :])
    grad_map = (own_grad[:, None, None, :] + spread).astype(jnp.bfloat16)
    return (grad_map, text_grad, group_sums)


def solution(mesh):
    dp_count, tile_count = mesh.devices.shape

    def run(section_map, *rest):
        rows_each = section_map.shape[1] // tile_count
        per_image = H // rows_each
        assert per_image & (per_image - 1) == 0
        split = Mesh(
            mesh.devices.reshape(dp_count, tile_count // per_image, per_image),
            ("dp", "img", "row"),
        )
        tiled = ("img", "row")
        placed = (
            P("dp", tiled, None, None),
            P(),
            P(),
            P(),
            P(),
            P(),
            P(),
            P("dp", None),
            P(),
            P(),
            P(),
        )
        return jax.shard_map(
            local,
            mesh=split,
            in_specs=placed,
            out_specs=(P("dp", tiled, None, None), P("dp", None), P()),
            check_vma=False,
        )(section_map, *rest)

    return run
```

```python
import jax
import jax.numpy as jnp
from jax import lax
from jax.sharding import Mesh
from jax.sharding import PartitionSpec as P

H = 32
W = 32
SOURCES = 32


LOGIT_SCALE = 10.0
LOGIT_BIAS = -5.0


def halo_rows(value, width):
    devices = lax.axis_size("row")
    up = [(i, i + 1) for i in range(devices - 1)]
    down = [(j, i) for i, j in up]
    length = value.shape[1]
    last = lax.slice_in_dim(value, length - width, length, axis=1)
    leading = lax.slice_in_dim(value, 0, width, axis=1)
    before = lax.ppermute(last, "row", up)
    after = lax.ppermute(leading, "row", down)
    return jnp.concatenate([before, value, after], axis=1)


def group_sum(value):
    devices = lax.axis_size("row")
    step = 1
    while step < devices:
        pairs = [(i, i ^ step) for i in range(devices)]
        value = value + lax.ppermute(value, "row", pairs)
        step *= 2
    return value


def gather_stages(value, axis, radices):
    place = 1
    devices = lax.axis_size(axis)
    at = lax.axis_index(axis)
    for radix in radices:
        digit = (at // place) % radix
        got = [value]
        for shift in range(1, radix):
            pairs = []
            for src in range(devices):
                d = (src // place) % radix
                pairs.append((src, src + ((d + shift) % radix - d) * place))
            got.append(lax.ppermute(value, axis, pairs))
        stacked = jnp.stack(got)
        order = (digit - jnp.arange(radix)) % radix
        value = jnp.take(stacked, order, axis=0)
        place *= radix
    return value.reshape((devices,) + value.shape[len(radices) :])


def radix_split(count):
    parts = []
    for radix in (3, 2):
        while count % radix == 0 and count > 1:
            parts.append(radix)
            count //= radix
    assert count == 1
    return parts


def cell_norm(values, gain):
    center = values - jnp.mean(values, axis=-1, keepdims=True)
    spread = jnp.mean(center * center, axis=-1, keepdims=True)
    return center * lax.rsqrt(spread + 1e-06) * gain


def unit_rows(values):
    return values * lax.rsqrt(jnp.sum(values * values, axis=-1, keepdims=True) + 1e-06)


def depthwise_rows(field, kernel):
    batch_rows, row_count, width, channels = field.shape
    framed = halo_rows(field, 3)
    framed = jnp.pad(framed, ((0, 0), (0, 0), (3, 3), (0, 0)))
    summed = jnp.zeros(field.shape, jnp.float32)
    for tap_row in range(7):
        for tap_col in range(7):
            window = framed[:, tap_row : tap_row + row_count, tap_col : tap_col + width, :].astype(
                jnp.float32
            )
            summed = summed + window * kernel[tap_row, tap_col].astype(jnp.float32)
    return summed


def local(
    section_map,
    dw_kernel,
    conv_bias,
    ln_gain,
    layer_scale,
    head_gain,
    head_weight,
    texts,
    positives,
    sources,
    numerators,
):
    batch_rows, row_count, width, channels = section_map.shape
    img_count = lax.axis_size("img")
    dp_count = lax.axis_size("dp")
    dp_at = lax.axis_index("dp")
    img_at = lax.axis_index("img")
    conved = depthwise_rows(section_map, dw_kernel) + conv_bias
    section_out = section_map.astype(jnp.float32) + layer_scale * cell_norm(conved, ln_gain)
    partial_value = jnp.sum(section_out, axis=(1, 2)) / (H * W)
    text_f = texts.astype(jnp.float32)
    text_vec = unit_rows(text_f).astype(jnp.bfloat16)
    text_count = texts.shape[0]
    text_vec, partial_value = lax.optimization_barrier((text_vec, partial_value))
    text_all = gather_stages(text_vec, "dp", radix_split(dp_count)).reshape(
        dp_count * text_count, -1
    )
    count = text_all.shape[0]
    pooled = group_sum(partial_value)
    head_in = cell_norm(pooled, head_gain).astype(jnp.bfloat16)
    embed = jnp.dot(head_in, head_weight, preferred_element_type=jnp.float32)
    image_vec = unit_rows(embed).astype(jnp.bfloat16)
    source_table = (sources[:, None] == jnp.arange(SOURCES)[None, :]).astype(jnp.float32)
    weights = (
        SOURCES
        * jnp.sum(source_table * numerators.astype(jnp.float32)[None, :], axis=1)
        / jnp.sum(numerators).astype(jnp.float32)
    )
    own_rows = (dp_at * batch_rows + jnp.arange(batch_rows)) * img_count + img_at
    own_logits = (
        LOGIT_SCALE * jnp.dot(image_vec, text_all.T, preferred_element_type=jnp.float32)
        + LOGIT_BIAS
    )
    own_labels = jnp.where(
        jnp.take(positives, own_rows)[:, None] == jnp.arange(count)[None, :], 1.0, -1.0
    ).astype(jnp.float32)
    own_weights = jnp.take(weights, own_rows)
    own_pair = (
        own_weights[:, None] * -own_labels * jax.nn.sigmoid(-own_labels * own_logits)
    ).astype(jnp.bfloat16)
    image_dir = LOGIT_SCALE * jnp.dot(own_pair, text_all, preferred_element_type=jnp.float32)
    embed_back = jax.vjp(unit_rows, embed)[1]
    embed_grad = embed_back(image_dir)[0].astype(jnp.bfloat16)
    head_grad = jnp.dot(embed_grad, head_weight.T, preferred_element_type=jnp.float32)
    pool_back = jax.vjp(lambda values: cell_norm(values, head_gain), pooled)[1]
    own_grad = pool_back(head_grad)[0]
    norm_back = jax.vjp(lambda values: cell_norm(values, ln_gain), conved)[1]
    seeded = jnp.broadcast_to((layer_scale * own_grad)[:, None, None, :], conved.shape)
    conv_grad = norm_back(seeded)[0].astype(jnp.bfloat16)
    image_vec, conv_grad = lax.optimization_barrier((image_vec, conv_grad))
    gathered = gather_stages(image_vec, "img", radix_split(img_count))
    gathered = gather_stages(gathered, "dp", radix_split(dp_count))
    image_all = jnp.transpose(gathered, (0, 2, 1, 3)).reshape(
        dp_count * batch_rows * img_count, -1
    )
    logits = (
        LOGIT_SCALE * jnp.dot(image_all, text_all.T, preferred_element_type=jnp.float32)
        + LOGIT_BIAS
    )
    labels = jnp.where(positives[:, None] == jnp.arange(count)[None, :], 1.0, -1.0).astype(
        jnp.float32
    )
    row_loss = lax.optimization_barrier(jnp.sum(jax.nn.softplus(-labels * logits), axis=1))
    group_sums = jnp.sum(source_table * (weights * row_loss)[:, None], axis=0)
    pair_grad = (weights[:, None] * -labels * jax.nn.sigmoid(-labels * logits)).astype(
        jnp.bfloat16
    )
    text_pair = lax.dynamic_slice_in_dim(pair_grad, dp_at * text_count, text_count, axis=1)
    text_dir = LOGIT_SCALE * lax.dot_general(
        text_pair, image_all, (((0,), (0,)), ((), ())), preferred_element_type=jnp.float32
    )
    text_back = jax.vjp(unit_rows, text_f)[1]
    text_grad = text_back(text_dir)[0]
    spread = depthwise_rows(conv_grad, dw_kernel[::-1, ::-1, :])
    grad_map = (own_grad[:, None, None, :] + spread).astype(jnp.bfloat16)
    return (grad_map, text_grad, group_sums)


def solution(mesh):
    dp_count, tile_count = mesh.devices.shape

    def run(section_map, *rest):
        rows_each = section_map.shape[1] // tile_count
        per_image = H // rows_each
        assert per_image & (per_image - 1) == 0
        split = Mesh(
            mesh.devices.reshape(dp_count, tile_count // per_image, per_image),
            ("dp", "img", "row"),
        )
        tiled = ("img", "row")
        placed = (
            P("dp", tiled, None, None),
            P(),
            P(),
            P(),
            P(),
            P(),
            P(),
            P("dp", None),
            P(),
            P(),
            P(),
        )
        return jax.shard_map(
            local,
            mesh=split,
            in_specs=placed,
            out_specs=(P("dp", tiled, None, None), P("dp", None), P()),
            check_vma=False,
        )(section_map, *rest)

    return run
```

```python
import jax
import jax.numpy as jnp
from jax import lax
from jax.sharding import Mesh
from jax.sharding import PartitionSpec as P

H = 32
W = 32
SOURCES = 32


LOGIT_SCALE = 10.0
LOGIT_BIAS = -5.0


def halo_rows(value, width):
    devices = lax.axis_size("row")
    up = [(i, i + 1) for i in range(devices - 1)]
    down = [(j, i) for i, j in up]
    length = value.shape[1]
    last = lax.slice_in_dim(value, length - width, length, axis=1)
    leading = lax.slice_in_dim(value, 0, width, axis=1)
    before = lax.ppermute(last, "row", up)
    after = lax.ppermute(leading, "row", down)
    return jnp.concatenate([before, value, after], axis=1)


def group_sum(value):
    devices = lax.axis_size("row")
    step = 1
    while step < devices:
        pairs = [(i, i ^ step) for i in range(devices)]
        value = value + lax.ppermute(value, "row", pairs)
        step *= 2
    return value


def gather_stages(value, axis, radices):
    place = 1
    devices = lax.axis_size(axis)
    at = lax.axis_index(axis)
    for radix in radices:
        digit = (at // place) % radix
        got = [value]
        for shift in range(1, radix):
            pairs = []
            for src in range(devices):
                d = (src // place) % radix
                pairs.append((src, src + ((d + shift) % radix - d) * place))
            got.append(lax.ppermute(value, axis, pairs))
        if radix == 2:
            first = digit == 0
            value = jnp.stack(
                [jnp.where(first, got[0], got[1]), jnp.where(first, got[1], got[0])]
            )
        else:
            stacked = jnp.stack(got)
            order = (digit - jnp.arange(radix)) % radix
            value = jnp.take(stacked, order, axis=0)
        place *= radix
    return value.reshape((devices,) + value.shape[len(radices) :])


def radix_split(count):
    parts = []
    for radix in (3, 2):
        while count % radix == 0 and count > 1:
            parts.append(radix)
            count //= radix
    assert count == 1
    return parts


def cell_norm(values, gain):
    center = values - jnp.mean(values, axis=-1, keepdims=True)
    spread = jnp.mean(center * center, axis=-1, keepdims=True)
    return center * lax.rsqrt(spread + 1e-06) * gain


def unit_rows(values):
    return values * lax.rsqrt(jnp.sum(values * values, axis=-1, keepdims=True) + 1e-06)


def depthwise_rows(field, kernel):
    batch_rows, row_count, width, channels = field.shape
    framed = halo_rows(field, 3)
    framed = jnp.pad(framed, ((0, 0), (0, 0), (3, 3), (0, 0)))
    summed = jnp.zeros(field.shape, jnp.float32)
    for tap_row in range(7):
        for tap_col in range(7):
            window = framed[:, tap_row : tap_row + row_count, tap_col : tap_col + width, :].astype(
                jnp.float32
            )
            summed = summed + window * kernel[tap_row, tap_col].astype(jnp.float32)
    return summed


def local(
    section_map,
    dw_kernel,
    conv_bias,
    ln_gain,
    layer_scale,
    head_gain,
    head_weight,
    texts,
    positives,
    sources,
    numerators,
):
    batch_rows, row_count, width, channels = section_map.shape
    img_count = lax.axis_size("img")
    dp_count = lax.axis_size("dp")
    dp_at = lax.axis_index("dp")
    img_at = lax.axis_index("img")
    conved = depthwise_rows(section_map, dw_kernel) + conv_bias
    section_out = section_map.astype(jnp.float32) + layer_scale * cell_norm(conved, ln_gain)
    partial_value = jnp.sum(section_out, axis=(1, 2)) / (H * W)
    pooled = group_sum(partial_value)
    head_in = cell_norm(pooled, head_gain).astype(jnp.bfloat16)
    embed = jnp.dot(head_in, head_weight, preferred_element_type=jnp.float32)
    image_vec = unit_rows(embed).astype(jnp.bfloat16)
    text_f = texts.astype(jnp.float32)
    text_vec = unit_rows(text_f).astype(jnp.bfloat16)
    text_count = texts.shape[0]
    share = text_count // img_count
    text_share = lax.dynamic_slice_in_dim(text_vec, img_at * share, share)
    payload = jnp.concatenate([image_vec, text_share], axis=0)
    gathered = gather_stages(payload, "img", radix_split(img_count))
    gathered = gather_stages(gathered, "dp", radix_split(dp_count))
    image_all = jnp.transpose(gathered[:, :, :batch_rows, :], (0, 2, 1, 3)).reshape(
        dp_count * batch_rows * img_count, -1
    )
    text_all = gathered[:, :, batch_rows:, :].reshape(dp_count * text_count, -1)
    count = text_all.shape[0]
    logits = (
        LOGIT_SCALE * jnp.dot(image_all, text_all.T, preferred_element_type=jnp.float32)
        + LOGIT_BIAS
    )
    labels = jnp.where(positives[:, None] == jnp.arange(count)[None, :], 1.0, -1.0).astype(
        jnp.float32
    )
    source_table = (sources[:, None] == jnp.arange(SOURCES)[None, :]).astype(jnp.float32)
    weights = (
        SOURCES
        * jnp.sum(source_table * numerators.astype(jnp.float32)[None, :], axis=1)
        / jnp.sum(numerators).astype(jnp.float32)
    )
    row_loss = lax.optimization_barrier(jnp.sum(jax.nn.softplus(-labels * logits), axis=1))
    group_sums = jnp.sum(source_table * (weights * row_loss)[:, None], axis=0)
    pair_grad = (weights[:, None] * -labels * jax.nn.sigmoid(-labels * logits)).astype(
        jnp.bfloat16
    )
    own_rows = (dp_at * batch_rows + jnp.arange(batch_rows)) * img_count + img_at
    own_pair = jnp.take(pair_grad, own_rows, axis=0)
    image_dir = LOGIT_SCALE * jnp.dot(own_pair, text_all, preferred_element_type=jnp.float32)
    text_pair = lax.dynamic_slice_in_dim(pair_grad, dp_at * text_count, text_count, axis=1)
    text_dir = LOGIT_SCALE * lax.dot_general(
        text_pair, image_all, (((0,), (0,)), ((), ())), preferred_element_type=jnp.float32
    )
    text_back = jax.vjp(unit_rows, text_f)[1]
    text_grad = text_back(text_dir)[0]
    embed_back = jax.vjp(unit_rows, embed)[1]
    embed_grad = embed_back(image_dir)[0].astype(jnp.bfloat16)
    head_grad = jnp.dot(embed_grad, head_weight.T, preferred_element_type=jnp.float32)
    pool_back = jax.vjp(lambda values: cell_norm(values, head_gain), pooled)[1]
    own_grad = pool_back(head_grad)[0]
    norm_back = jax.vjp(lambda values: cell_norm(values, ln_gain), conved)[1]
    seeded = jnp.broadcast_to((layer_scale * own_grad)[:, None, None, :], conved.shape)
    conv_grad = norm_back(seeded)[0].astype(jnp.bfloat16)
    spread = depthwise_rows(conv_grad, dw_kernel[::-1, ::-1, :])
    grad_map = (own_grad[:, None, None, :] + spread).astype(jnp.bfloat16)
    return (grad_map, text_grad, group_sums)


def solution(mesh):
    dp_count, tile_count = mesh.devices.shape

    def run(section_map, *rest):
        rows_each = section_map.shape[1] // tile_count
        per_image = H // rows_each
        assert per_image & (per_image - 1) == 0
        split = Mesh(
            mesh.devices.reshape(dp_count, tile_count // per_image, per_image),
            ("dp", "img", "row"),
        )
        tiled = ("img", "row")
        placed = (
            P("dp", tiled, None, None),
            P(),
            P(),
            P(),
            P(),
            P(),
            P(),
            P("dp", None),
            P(),
            P(),
            P(),
        )
        return jax.shard_map(
            local,
            mesh=split,
            in_specs=placed,
            out_specs=(P("dp", tiled, None, None), P("dp", None), P()),
            check_vma=False,
        )(section_map, *rest)

    return run
```

```python
import jax
import jax.numpy as jnp
from jax import lax
from jax.sharding import Mesh
from jax.sharding import PartitionSpec as P

H = 32
W = 32
SOURCES = 32


LOGIT_SCALE = 10.0
LOGIT_BIAS = -5.0


def halo_rows(value, width):
    devices = lax.axis_size("row")
    up = [(i, i + 1) for i in range(devices - 1)]
    down = [(j, i) for i, j in up]
    length = value.shape[1]
    last = lax.slice_in_dim(value, length - width, length, axis=1)
    leading = lax.slice_in_dim(value, 0, width, axis=1)
    before = lax.ppermute(last, "row", up)
    after = lax.ppermute(leading, "row", down)
    return jnp.concatenate([before, value, after], axis=1)


def group_sum(value):
    devices = lax.axis_size("row")
    step = 1
    while step < devices:
        pairs = [(i, i ^ step) for i in range(devices)]
        value = value + lax.ppermute(value, "row", pairs)
        step *= 2
    return value


def gather_stages(value, axis, radices):
    place = 1
    devices = lax.axis_size(axis)
    at = lax.axis_index(axis)
    for radix in radices:
        digit = (at // place) % radix
        got = [value]
        for shift in range(1, radix):
            pairs = []
            for src in range(devices):
                d = (src // place) % radix
                pairs.append((src, src + ((d + shift) % radix - d) * place))
            got.append(lax.ppermute(value, axis, pairs))
        if radix == 2:
            first = digit == 0
            value = jnp.stack(
                [jnp.where(first, got[0], got[1]), jnp.where(first, got[1], got[0])]
            )
        else:
            stacked = jnp.stack(got)
            order = (digit - jnp.arange(radix)) % radix
            value = jnp.take(stacked, order, axis=0)
        place *= radix
    return value.reshape((devices,) + value.shape[len(radices) :])


def radix_split(count):
    parts = []
    for radix in (3, 2):
        while count % radix == 0 and count > 1:
            parts.append(radix)
            count //= radix
    assert count == 1
    return parts


def cell_norm(values, gain):
    center = values - jnp.mean(values, axis=-1, keepdims=True)
    spread = jnp.mean(center * center, axis=-1, keepdims=True)
    return center * lax.rsqrt(spread + 1e-06) * gain


def unit_rows(values):
    return values * lax.rsqrt(jnp.sum(values * values, axis=-1, keepdims=True) + 1e-06)


def depthwise_rows(field, kernel):
    batch_rows, row_count, width, channels = field.shape
    framed = halo_rows(field, 3)
    framed = jnp.pad(framed, ((0, 0), (0, 0), (3, 3), (0, 0)))
    summed = jnp.zeros(field.shape, jnp.float32)
    for tap_row in range(7):
        for tap_col in range(7):
            window = framed[:, tap_row : tap_row + row_count, tap_col : tap_col + width, :].astype(
                jnp.float32
            )
            summed = summed + window * kernel[tap_row, tap_col].astype(jnp.float32)
    return summed


def local(
    section_map,
    dw_kernel,
    conv_bias,
    ln_gain,
    layer_scale,
    head_gain,
    head_weight,
    texts,
    positives,
    sources,
    numerators,
):
    batch_rows, row_count, width, channels = section_map.shape
    img_count = lax.axis_size("img")
    dp_count = lax.axis_size("dp")
    dp_at = lax.axis_index("dp")
    img_at = lax.axis_index("img")
    conved = depthwise_rows(section_map, dw_kernel) + conv_bias
    section_out = section_map.astype(jnp.float32) + layer_scale * cell_norm(conved, ln_gain)
    partial_value = jnp.sum(section_out, axis=(1, 2)) / (H * W)
    pooled = group_sum(partial_value)
    head_in = cell_norm(pooled, head_gain).astype(jnp.bfloat16)
    embed = jnp.dot(head_in, head_weight, preferred_element_type=jnp.float32)
    image_vec = unit_rows(embed).astype(jnp.bfloat16)
    text_f = texts.astype(jnp.float32)
    text_vec = unit_rows(text_f).astype(jnp.bfloat16)
    text_count = texts.shape[0]
    share = text_count // img_count
    text_share = lax.dynamic_slice_in_dim(text_vec, img_at * share, share)
    payload = jnp.concatenate([image_vec, text_share], axis=0)
    gathered = gather_stages(payload, "img", radix_split(img_count))
    gathered = gather_stages(gathered, "dp", radix_split(dp_count))
    image_all = gathered[:, :, :batch_rows, :].reshape(dp_count * img_count * batch_rows, -1)
    text_all = gathered[:, :, batch_rows:, :].reshape(dp_count * text_count, -1)
    count = text_all.shape[0]

    def in_gathered_order(vector):
        return jnp.transpose(vector.reshape(dp_count, batch_rows, img_count), (0, 2, 1)).reshape(-1)

    positives_g = in_gathered_order(positives)
    sources_g = in_gathered_order(sources)
    logits = (
        LOGIT_SCALE * jnp.dot(image_all, text_all.T, preferred_element_type=jnp.float32)
        + LOGIT_BIAS
    )
    labels = jnp.where(positives_g[:, None] == jnp.arange(count)[None, :], 1.0, -1.0).astype(
        jnp.float32
    )
    source_table = (sources_g[:, None] == jnp.arange(SOURCES)[None, :]).astype(jnp.float32)
    weights = (
        SOURCES
        * jnp.sum(source_table * numerators.astype(jnp.float32)[None, :], axis=1)
        / jnp.sum(numerators).astype(jnp.float32)
    )
    pair_grad = (weights[:, None] * -labels * jax.nn.sigmoid(-labels * logits)).astype(
        jnp.bfloat16
    )
    own_at = (dp_at * img_count + img_at) * batch_rows
    own_pair = lax.dynamic_slice_in_dim(pair_grad, own_at, batch_rows, axis=0)
    image_dir = LOGIT_SCALE * jnp.dot(own_pair, text_all, preferred_element_type=jnp.float32)
    embed_back = jax.vjp(unit_rows, embed)[1]
    embed_grad = embed_back(image_dir)[0].astype(jnp.bfloat16)
    head_grad = jnp.dot(embed_grad, head_weight.T, preferred_element_type=jnp.float32)
    pool_back = jax.vjp(lambda values: cell_norm(values, head_gain), pooled)[1]
    own_grad = pool_back(head_grad)[0]
    norm_back = jax.vjp(lambda values: cell_norm(values, ln_gain), conved)[1]
    seeded = jnp.broadcast_to((layer_scale * own_grad)[:, None, None, :], conved.shape)
    conv_grad = norm_back(seeded)[0].astype(jnp.bfloat16)
    logits, pair_grad, conv_grad = lax.optimization_barrier((logits, pair_grad, conv_grad))
    row_loss = lax.optimization_barrier(jnp.sum(jax.nn.softplus(-labels * logits), axis=1))
    group_sums = jnp.sum(source_table * (weights * row_loss)[:, None], axis=0)
    text_pair = lax.dynamic_slice_in_dim(pair_grad, dp_at * text_count, text_count, axis=1)
    text_dir = LOGIT_SCALE * lax.dot_general(
        text_pair, image_all, (((0,), (0,)), ((), ())), preferred_element_type=jnp.float32
    )
    text_back = jax.vjp(unit_rows, text_f)[1]
    text_grad = text_back(text_dir)[0]
    spread = depthwise_rows(conv_grad, dw_kernel[::-1, ::-1, :])
    grad_map = (own_grad[:, None, None, :] + spread).astype(jnp.bfloat16)
    return (grad_map, text_grad, group_sums)


def solution(mesh):
    dp_count, tile_count = mesh.devices.shape

    def run(section_map, *rest):
        rows_each = section_map.shape[1] // tile_count
        per_image = H // rows_each
        assert per_image & (per_image - 1) == 0
        split = Mesh(
            mesh.devices.reshape(dp_count, tile_count // per_image, per_image),
            ("dp", "img", "row"),
        )
        tiled = ("img", "row")
        placed = (
            P("dp", tiled, None, None),
            P(),
            P(),
            P(),
            P(),
            P(),
            P(),
            P("dp", None),
            P(),
            P(),
            P(),
        )
        return jax.shard_map(
            local,
            mesh=split,
            in_specs=placed,
            out_specs=(P("dp", tiled, None, None), P("dp", None), P()),
            check_vma=False,
        )(section_map, *rest)

    return run
```

```python
import jax
import jax.numpy as jnp
from jax import lax
from jax.sharding import Mesh
from jax.sharding import PartitionSpec as P

H = 32
W = 32
SOURCES = 32


LOGIT_SCALE = 10.0
LOGIT_BIAS = -5.0


def halo_rows(value, width):
    devices = lax.axis_size("row")
    up = [(i, i + 1) for i in range(devices - 1)]
    down = [(j, i) for i, j in up]
    length = value.shape[1]
    last = lax.slice_in_dim(value, length - width, length, axis=1)
    leading = lax.slice_in_dim(value, 0, width, axis=1)
    before = lax.ppermute(last, "row", up)
    after = lax.ppermute(leading, "row", down)
    return jnp.concatenate([before, value, after], axis=1)


def group_sum(value):
    devices = lax.axis_size("row")
    step = 1
    while step < devices:
        pairs = [(i, i ^ step) for i in range(devices)]
        value = value + lax.ppermute(value, "row", pairs)
        step *= 2
    return value


def gather_stages(value, axis, radices):
    place = 1
    devices = lax.axis_size(axis)
    at = lax.axis_index(axis)
    for radix in radices:
        digit = (at // place) % radix
        got = [value]
        for shift in range(1, radix):
            pairs = []
            for src in range(devices):
                d = (src // place) % radix
                pairs.append((src, src + ((d + shift) % radix - d) * place))
            got.append(lax.ppermute(value, axis, pairs))
        if radix == 2:
            first = digit == 0
            value = jnp.stack(
                [jnp.where(first, got[0], got[1]), jnp.where(first, got[1], got[0])]
            )
        else:
            stacked = jnp.stack(got)
            order = (digit - jnp.arange(radix)) % radix
            value = jnp.take(stacked, order, axis=0)
        place *= radix
    return value.reshape((devices,) + value.shape[len(radices) :])


def radix_split(count):
    parts = []
    for radix in (3, 2):
        while count % radix == 0 and count > 1:
            parts.append(radix)
            count //= radix
    assert count == 1
    return parts


def cell_norm(values, gain):
    center = values - jnp.mean(values, axis=-1, keepdims=True)
    spread = jnp.mean(center * center, axis=-1, keepdims=True)
    return center * lax.rsqrt(spread + 1e-06) * gain


def unit_rows(values):
    return values * lax.rsqrt(jnp.sum(values * values, axis=-1, keepdims=True) + 1e-06)


def depthwise_rows(field, kernel, beside=None):
    batch_rows, row_count, width, channels = field.shape
    framed = halo_rows(field, 3)
    framed, beside = lax.optimization_barrier((framed, beside))
    framed = jnp.pad(framed, ((0, 0), (0, 0), (3, 3), (0, 0)))
    summed = jnp.zeros(field.shape, jnp.float32)
    for tap_row in range(7):
        for tap_col in range(7):
            window = framed[:, tap_row : tap_row + row_count, tap_col : tap_col + width, :].astype(
                jnp.float32
            )
            summed = summed + window * kernel[tap_row, tap_col].astype(jnp.float32)
    return summed, beside


def local(
    section_map,
    dw_kernel,
    conv_bias,
    ln_gain,
    layer_scale,
    head_gain,
    head_weight,
    texts,
    positives,
    sources,
    numerators,
):
    batch_rows, row_count, width, channels = section_map.shape
    img_count = lax.axis_size("img")
    dp_count = lax.axis_size("dp")
    dp_at = lax.axis_index("dp")
    img_at = lax.axis_index("img")
    text_f = texts.astype(jnp.float32)
    text_vec = unit_rows(text_f).astype(jnp.bfloat16)
    text_count = texts.shape[0]
    share = text_count // img_count
    text_share = lax.dynamic_slice_in_dim(text_vec, img_at * share, share)
    count = dp_count * text_count

    def in_gathered_order(vector):
        return jnp.transpose(vector.reshape(dp_count, batch_rows, img_count), (0, 2, 1)).reshape(-1)

    positives_g = in_gathered_order(positives)
    sources_g = in_gathered_order(sources)
    labels = jnp.where(positives_g[:, None] == jnp.arange(count)[None, :], 1.0, -1.0).astype(
        jnp.float32
    )
    source_table = (sources_g[:, None] == jnp.arange(SOURCES)[None, :]).astype(jnp.float32)
    weights = (
        SOURCES
        * jnp.sum(source_table * numerators.astype(jnp.float32)[None, :], axis=1)
        / jnp.sum(numerators).astype(jnp.float32)
    )
    early = (text_share, labels, source_table, weights)
    conved, early = depthwise_rows(section_map, dw_kernel, early)
    text_share, labels, source_table, weights = early
    conved = conved + conv_bias
    section_out = section_map.astype(jnp.float32) + layer_scale * cell_norm(conved, ln_gain)
    partial_value = jnp.sum(section_out, axis=(1, 2)) / (H * W)
    pooled = group_sum(partial_value)
    head_in = cell_norm(pooled, head_gain).astype(jnp.bfloat16)
    embed = jnp.dot(head_in, head_weight, preferred_element_type=jnp.float32)
    image_vec = unit_rows(embed).astype(jnp.bfloat16)
    payload = jnp.concatenate([image_vec, text_share], axis=0)
    gathered = gather_stages(payload, "img", radix_split(img_count))
    gathered = gather_stages(gathered, "dp", radix_split(dp_count))
    image_all = gathered[:, :, :batch_rows, :].reshape(dp_count * img_count * batch_rows, -1)
    text_all = gathered[:, :, batch_rows:, :].reshape(dp_count * text_count, -1)
    logits = (
        LOGIT_SCALE * jnp.dot(image_all, text_all.T, preferred_element_type=jnp.float32)
        + LOGIT_BIAS
    )
    pair_grad = (weights[:, None] * -labels * jax.nn.sigmoid(-labels * logits)).astype(
        jnp.bfloat16
    )
    own_at = (dp_at * img_count + img_at) * batch_rows
    own_pair = lax.dynamic_slice_in_dim(pair_grad, own_at, batch_rows, axis=0)
    image_dir = LOGIT_SCALE * jnp.dot(own_pair, text_all, preferred_element_type=jnp.float32)
    embed_back = jax.vjp(unit_rows, embed)[1]
    embed_grad = embed_back(image_dir)[0].astype(jnp.bfloat16)
    head_grad = jnp.dot(embed_grad, head_weight.T, preferred_element_type=jnp.float32)
    pool_back = jax.vjp(lambda values: cell_norm(values, head_gain), pooled)[1]
    own_grad = pool_back(head_grad)[0]
    norm_back = jax.vjp(lambda values: cell_norm(values, ln_gain), conved)[1]
    seeded = jnp.broadcast_to((layer_scale * own_grad)[:, None, None, :], conved.shape)
    conv_grad = norm_back(seeded)[0].astype(jnp.bfloat16)
    logits, pair_grad, conv_grad = lax.optimization_barrier((logits, pair_grad, conv_grad))
    row_loss = lax.optimization_barrier(jnp.sum(jax.nn.softplus(-labels * logits), axis=1))
    group_sums = jnp.sum(source_table * (weights * row_loss)[:, None], axis=0)
    text_pair = lax.dynamic_slice_in_dim(pair_grad, dp_at * text_count, text_count, axis=1)
    text_dir = LOGIT_SCALE * lax.dot_general(
        text_pair, image_all, (((0,), (0,)), ((), ())), preferred_element_type=jnp.float32
    )
    text_back = jax.vjp(unit_rows, text_f)[1]
    text_grad = text_back(text_dir)[0]
    spread = depthwise_rows(conv_grad, dw_kernel[::-1, ::-1, :])[0]
    grad_map = (own_grad[:, None, None, :] + spread).astype(jnp.bfloat16)
    return (grad_map, text_grad, group_sums)


def solution(mesh):
    dp_count, tile_count = mesh.devices.shape

    def run(section_map, *rest):
        rows_each = section_map.shape[1] // tile_count
        per_image = H // rows_each
        assert per_image & (per_image - 1) == 0
        split = Mesh(
            mesh.devices.reshape(dp_count, tile_count // per_image, per_image),
            ("dp", "img", "row"),
        )
        tiled = ("img", "row")
        placed = (
            P("dp", tiled, None, None),
            P(),
            P(),
            P(),
            P(),
            P(),
            P(),
            P("dp", None),
            P(),
            P(),
            P(),
        )
        return jax.shard_map(
            local,
            mesh=split,
            in_specs=placed,
            out_specs=(P("dp", tiled, None, None), P("dp", None), P()),
            check_vma=False,
        )(section_map, *rest)

    return run
```

```python
import jax
import jax.numpy as jnp
from jax import lax
from jax.sharding import Mesh
from jax.sharding import PartitionSpec as P

H = 32
W = 32
SOURCES = 32


LOGIT_SCALE = 10.0
LOGIT_BIAS = -5.0


def halo_rows(value, width):
    devices = lax.axis_size("row")
    up = [(i, i + 1) for i in range(devices - 1)]
    down = [(j, i) for i, j in up]
    length = value.shape[1]
    last = lax.slice_in_dim(value, length - width, length, axis=1)
    leading = lax.slice_in_dim(value, 0, width, axis=1)
    before = lax.ppermute(last, "row", up)
    after = lax.ppermute(leading, "row", down)
    return jnp.concatenate([before, value, after], axis=1)


def group_sum(value):
    devices = lax.axis_size("row")
    step = 1
    while step < devices:
        pairs = [(i, i ^ step) for i in range(devices)]
        value = value + lax.ppermute(value, "row", pairs)
        step *= 2
    return value


def gather_stages(value, axis, radices):
    place = 1
    devices = lax.axis_size(axis)
    at = lax.axis_index(axis)
    for radix in radices:
        digit = (at // place) % radix
        got = [value]
        for shift in range(1, radix):
            pairs = []
            for src in range(devices):
                d = (src // place) % radix
                pairs.append((src, src + ((d + shift) % radix - d) * place))
            got.append(lax.ppermute(value, axis, pairs))
        if radix == 2:
            first = digit == 0
            value = jnp.stack(
                [jnp.where(first, got[0], got[1]), jnp.where(first, got[1], got[0])]
            )
        else:
            stacked = jnp.stack(got)
            order = (digit - jnp.arange(radix)) % radix
            value = jnp.take(stacked, order, axis=0)
        place *= radix
    return value.reshape((devices,) + value.shape[len(radices) :])


def radix_split(count):
    parts = []
    for radix in (2, 3):
        while count % radix == 0 and count > 1:
            parts.append(radix)
            count //= radix
    assert count == 1
    return parts


def cell_norm(values, gain):
    center = values - jnp.mean(values, axis=-1, keepdims=True)
    spread = jnp.mean(center * center, axis=-1, keepdims=True)
    return center * lax.rsqrt(spread + 1e-06) * gain


def unit_rows(values):
    return values * lax.rsqrt(jnp.sum(values * values, axis=-1, keepdims=True) + 1e-06)


def depthwise_rows(field, kernel, beside=None):
    batch_rows, row_count, width, channels = field.shape
    framed = halo_rows(field, 3)
    framed, beside = lax.optimization_barrier((framed, beside))
    framed = jnp.pad(framed, ((0, 0), (0, 0), (3, 3), (0, 0)))
    summed = jnp.zeros(field.shape, jnp.float32)
    for tap_row in range(7):
        for tap_col in range(7):
            window = framed[:, tap_row : tap_row + row_count, tap_col : tap_col + width, :].astype(
                jnp.float32
            )
            summed = summed + window * kernel[tap_row, tap_col].astype(jnp.float32)
    return summed, beside


def local(
    section_map,
    dw_kernel,
    conv_bias,
    ln_gain,
    layer_scale,
    head_gain,
    head_weight,
    texts,
    positives,
    sources,
    numerators,
):
    batch_rows, row_count, width, channels = section_map.shape
    img_count = lax.axis_size("img")
    dp_count = lax.axis_size("dp")
    dp_at = lax.axis_index("dp")
    img_at = lax.axis_index("img")
    text_f = texts.astype(jnp.float32)
    text_vec = unit_rows(text_f).astype(jnp.bfloat16)
    text_count = texts.shape[0]
    share = text_count // img_count
    text_share = lax.dynamic_slice_in_dim(text_vec, img_at * share, share)
    count = dp_count * text_count

    def in_gathered_order(vector):
        return jnp.transpose(vector.reshape(dp_count, batch_rows, img_count), (0, 2, 1)).reshape(-1)

    positives_g = in_gathered_order(positives)
    sources_g = in_gathered_order(sources)
    labels = jnp.where(positives_g[:, None] == jnp.arange(count)[None, :], 1.0, -1.0).astype(
        jnp.float32
    )
    source_table = (sources_g[:, None] == jnp.arange(SOURCES)[None, :]).astype(jnp.float32)
    weights = (
        SOURCES
        * jnp.sum(source_table * numerators.astype(jnp.float32)[None, :], axis=1)
        / jnp.sum(numerators).astype(jnp.float32)
    )
    early = (text_share, labels, source_table, weights)
    conved, early = depthwise_rows(section_map, dw_kernel, early)
    text_share, labels, source_table, weights = early
    conved = conved + conv_bias
    section_out = section_map.astype(jnp.float32) + layer_scale * cell_norm(conved, ln_gain)
    partial_value = jnp.sum(section_out, axis=(1, 2)) / (H * W)
    pooled = group_sum(partial_value)
    head_in = cell_norm(pooled, head_gain).astype(jnp.bfloat16)
    embed = jnp.dot(head_in, head_weight, preferred_element_type=jnp.float32)
    image_vec = unit_rows(embed).astype(jnp.bfloat16)
    payload = jnp.concatenate([image_vec, text_share], axis=0)
    gathered = gather_stages(payload, "img", radix_split(img_count))
    gathered = gather_stages(gathered, "dp", radix_split(dp_count))
    image_all = gathered[:, :, :batch_rows, :].reshape(dp_count * img_count * batch_rows, -1)
    text_all = gathered[:, :, batch_rows:, :].reshape(dp_count * text_count, -1)
    logits = (
        LOGIT_SCALE * jnp.dot(image_all, text_all.T, preferred_element_type=jnp.float32)
        + LOGIT_BIAS
    )
    pair_grad = (weights[:, None] * -labels * jax.nn.sigmoid(-labels * logits)).astype(
        jnp.bfloat16
    )
    own_at = (dp_at * img_count + img_at) * batch_rows
    own_pair = lax.dynamic_slice_in_dim(pair_grad, own_at, batch_rows, axis=0)
    image_dir = LOGIT_SCALE * jnp.dot(own_pair, text_all, preferred_element_type=jnp.float32)
    embed_back = jax.vjp(unit_rows, embed)[1]
    embed_grad = embed_back(image_dir)[0].astype(jnp.bfloat16)
    head_grad = jnp.dot(embed_grad, head_weight.T, preferred_element_type=jnp.float32)
    pool_back = jax.vjp(lambda values: cell_norm(values, head_gain), pooled)[1]
    own_grad = pool_back(head_grad)[0]
    norm_back = jax.vjp(lambda values: cell_norm(values, ln_gain), conved)[1]
    seeded = jnp.broadcast_to((layer_scale * own_grad)[:, None, None, :], conved.shape)
    conv_grad = norm_back(seeded)[0].astype(jnp.bfloat16)
    logits, pair_grad, conv_grad = lax.optimization_barrier((logits, pair_grad, conv_grad))
    row_loss = lax.optimization_barrier(jnp.sum(jax.nn.softplus(-labels * logits), axis=1))
    group_sums = jnp.sum(source_table * (weights * row_loss)[:, None], axis=0)
    text_pair = lax.dynamic_slice_in_dim(pair_grad, dp_at * text_count, text_count, axis=1)
    text_dir = LOGIT_SCALE * lax.dot_general(
        text_pair, image_all, (((0,), (0,)), ((), ())), preferred_element_type=jnp.float32
    )
    text_back = jax.vjp(unit_rows, text_f)[1]
    text_grad = text_back(text_dir)[0]
    spread = depthwise_rows(conv_grad, dw_kernel[::-1, ::-1, :])[0]
    grad_map = (own_grad[:, None, None, :] + spread).astype(jnp.bfloat16)
    return (grad_map, text_grad, group_sums)


def solution(mesh):
    dp_count, tile_count = mesh.devices.shape

    def run(section_map, *rest):
        rows_each = section_map.shape[1] // tile_count
        per_image = H // rows_each
        assert per_image & (per_image - 1) == 0
        split = Mesh(
            mesh.devices.reshape(dp_count, tile_count // per_image, per_image),
            ("dp", "img", "row"),
        )
        tiled = ("img", "row")
        placed = (
            P("dp", tiled, None, None),
            P(),
            P(),
            P(),
            P(),
            P(),
            P(),
            P("dp", None),
            P(),
            P(),
            P(),
        )
        return jax.shard_map(
            local,
            mesh=split,
            in_specs=placed,
            out_specs=(P("dp", tiled, None, None), P("dp", None), P()),
            check_vma=False,
        )(section_map, *rest)

    return run
```

```python
import jax
import jax.numpy as jnp
from jax import lax
from jax.sharding import Mesh
from jax.sharding import PartitionSpec as P

H = 32
W = 32
SOURCES = 32


LOGIT_SCALE = 10.0
LOGIT_BIAS = -5.0


def halo_rows(value, width):
    devices = lax.axis_size("row")
    up = [(i, i + 1) for i in range(devices - 1)]
    down = [(j, i) for i, j in up]
    length = value.shape[1]
    last = lax.slice_in_dim(value, length - width, length, axis=1)
    leading = lax.slice_in_dim(value, 0, width, axis=1)
    before = lax.ppermute(last, "row", up)
    after = lax.ppermute(leading, "row", down)
    return jnp.concatenate([before, value, after], axis=1)


def group_sum(value):
    devices = lax.axis_size("row")
    step = 1
    while step < devices:
        pairs = [(i, i ^ step) for i in range(devices)]
        value = value + lax.ppermute(value, "row", pairs)
        step *= 2
    return value


def gather_stages(value, axis, radices):
    devices = lax.axis_size(axis)
    at = lax.axis_index(axis)
    places = []
    place = 1
    for radix in radices:
        places.append(place)
        place *= radix
    for stage, (radix, place) in enumerate(reversed(list(zip(radices, places)))):
        digit = (at // place) % radix
        got = [value]
        for shift in range(1, radix):
            pairs = []
            for src in range(devices):
                d = (src // place) % radix
                pairs.append((src, src + ((d + shift) % radix - d) * place))
            got.append(lax.ppermute(value, axis, pairs))
        if radix == 2:
            first = digit == 0
            value = jnp.stack(
                [jnp.where(first, got[0], got[1]), jnp.where(first, got[1], got[0])], axis=stage
            )
        else:
            stacked = jnp.stack(got, axis=stage)
            order = (digit - jnp.arange(radix)) % radix
            value = jnp.take(stacked, order, axis=stage)
    return value.reshape((devices,) + value.shape[len(radices) :])


def radix_split(count):
    parts = []
    for radix in (3, 2):
        while count % radix == 0 and count > 1:
            parts.append(radix)
            count //= radix
    assert count == 1
    return parts


def cell_norm(values, gain):
    center = values - jnp.mean(values, axis=-1, keepdims=True)
    spread = jnp.mean(center * center, axis=-1, keepdims=True)
    return center * lax.rsqrt(spread + 1e-06) * gain


def unit_rows(values):
    return values * lax.rsqrt(jnp.sum(values * values, axis=-1, keepdims=True) + 1e-06)


def depthwise_rows(field, kernel, beside=None):
    batch_rows, row_count, width, channels = field.shape
    framed = halo_rows(field, 3)
    framed, beside = lax.optimization_barrier((framed, beside))
    framed = jnp.pad(framed, ((0, 0), (0, 0), (3, 3), (0, 0)))
    summed = jnp.zeros(field.shape, jnp.float32)
    for tap_row in range(7):
        for tap_col in range(7):
            window = framed[:, tap_row : tap_row + row_count, tap_col : tap_col + width, :].astype(
                jnp.float32
            )
            summed = summed + window * kernel[tap_row, tap_col].astype(jnp.float32)
    return summed, beside


def local(
    section_map,
    dw_kernel,
    conv_bias,
    ln_gain,
    layer_scale,
    head_gain,
    head_weight,
    texts,
    positives,
    sources,
    numerators,
):
    batch_rows, row_count, width, channels = section_map.shape
    img_count = lax.axis_size("img")
    dp_count = lax.axis_size("dp")
    dp_at = lax.axis_index("dp")
    img_at = lax.axis_index("img")
    text_f = texts.astype(jnp.float32)
    text_vec = unit_rows(text_f).astype(jnp.bfloat16)
    text_count = texts.shape[0]
    share = text_count // img_count
    text_share = lax.dynamic_slice_in_dim(text_vec, img_at * share, share)
    count = dp_count * text_count

    def in_gathered_order(vector):
        return jnp.transpose(vector.reshape(dp_count, batch_rows, img_count), (0, 2, 1)).reshape(-1)

    positives_g = in_gathered_order(positives)
    sources_g = in_gathered_order(sources)
    labels = jnp.where(positives_g[:, None] == jnp.arange(count)[None, :], 1.0, -1.0).astype(
        jnp.float32
    )
    source_table = (sources_g[:, None] == jnp.arange(SOURCES)[None, :]).astype(jnp.float32)
    weights = (
        SOURCES
        * jnp.sum(source_table * numerators.astype(jnp.float32)[None, :], axis=1)
        / jnp.sum(numerators).astype(jnp.float32)
    )
    early = (text_share, labels, source_table, weights)
    conved, early = depthwise_rows(section_map, dw_kernel, early)
    text_share, labels, source_table, weights = early
    conved = conved + conv_bias
    section_out = section_map.astype(jnp.float32) + layer_scale * cell_norm(conved, ln_gain)
    partial_value = jnp.sum(section_out, axis=(1, 2)) / (H * W)
    pooled = group_sum(partial_value)
    head_in = cell_norm(pooled, head_gain).astype(jnp.bfloat16)
    embed = jnp.dot(head_in, head_weight, preferred_element_type=jnp.float32)
    image_vec = unit_rows(embed).astype(jnp.bfloat16)
    payload = jnp.concatenate([image_vec, text_share], axis=0)
    gathered = gather_stages(payload, "img", radix_split(img_count))
    gathered = gather_stages(gathered, "dp", radix_split(dp_count))
    image_all = gathered[:, :, :batch_rows, :].reshape(dp_count * img_count * batch_rows, -1)
    text_all = gathered[:, :, batch_rows:, :].reshape(dp_count * text_count, -1)
    logits = (
        LOGIT_SCALE * jnp.dot(image_all, text_all.T, preferred_element_type=jnp.float32)
        + LOGIT_BIAS
    )
    pair_grad = (weights[:, None] * -labels * jax.nn.sigmoid(-labels * logits)).astype(
        jnp.bfloat16
    )
    own_at = (dp_at * img_count + img_at) * batch_rows
    own_pair = lax.dynamic_slice_in_dim(pair_grad, own_at, batch_rows, axis=0)
    image_dir = LOGIT_SCALE * jnp.dot(own_pair, text_all, preferred_element_type=jnp.float32)
    embed_back = jax.vjp(unit_rows, embed)[1]
    embed_grad = embed_back(image_dir)[0].astype(jnp.bfloat16)
    head_grad = jnp.dot(embed_grad, head_weight.T, preferred_element_type=jnp.float32)
    pool_back = jax.vjp(lambda values: cell_norm(values, head_gain), pooled)[1]
    own_grad = pool_back(head_grad)[0]
    norm_back = jax.vjp(lambda values: cell_norm(values, ln_gain), conved)[1]
    seeded = jnp.broadcast_to((layer_scale * own_grad)[:, None, None, :], conved.shape)
    conv_grad = norm_back(seeded)[0].astype(jnp.bfloat16)
    logits, pair_grad, conv_grad = lax.optimization_barrier((logits, pair_grad, conv_grad))
    row_loss = lax.optimization_barrier(jnp.sum(jax.nn.softplus(-labels * logits), axis=1))
    group_sums = jnp.sum(source_table * (weights * row_loss)[:, None], axis=0)
    text_pair = lax.dynamic_slice_in_dim(pair_grad, dp_at * text_count, text_count, axis=1)
    text_dir = LOGIT_SCALE * lax.dot_general(
        text_pair, image_all, (((0,), (0,)), ((), ())), preferred_element_type=jnp.float32
    )
    text_back = jax.vjp(unit_rows, text_f)[1]
    text_grad = text_back(text_dir)[0]
    spread = depthwise_rows(conv_grad, dw_kernel[::-1, ::-1, :])[0]
    grad_map = (own_grad[:, None, None, :] + spread).astype(jnp.bfloat16)
    return (grad_map, text_grad, group_sums)


def solution(mesh):
    dp_count, tile_count = mesh.devices.shape

    def run(section_map, *rest):
        rows_each = section_map.shape[1] // tile_count
        per_image = H // rows_each
        assert per_image & (per_image - 1) == 0
        split = Mesh(
            mesh.devices.reshape(dp_count, tile_count // per_image, per_image),
            ("dp", "img", "row"),
        )
        tiled = ("img", "row")
        placed = (
            P("dp", tiled, None, None),
            P(),
            P(),
            P(),
            P(),
            P(),
            P(),
            P("dp", None),
            P(),
            P(),
            P(),
        )
        return jax.shard_map(
            local,
            mesh=split,
            in_specs=placed,
            out_specs=(P("dp", tiled, None, None), P("dp", None), P()),
            check_vma=False,
        )(section_map, *rest)

    return run
```

```python
import jax
import jax.numpy as jnp
from jax import lax
from jax.sharding import Mesh
from jax.sharding import PartitionSpec as P

H = 32
W = 32
SOURCES = 32


LOGIT_SCALE = 10.0
LOGIT_BIAS = -5.0


def halo_rows(value, width):
    devices = lax.axis_size("row")
    up = [(i, i + 1) for i in range(devices - 1)]
    down = [(j, i) for i, j in up]
    length = value.shape[1]
    last = lax.slice_in_dim(value, length - width, length, axis=1)
    leading = lax.slice_in_dim(value, 0, width, axis=1)
    before = lax.ppermute(last, "row", up)
    after = lax.ppermute(leading, "row", down)
    return jnp.concatenate([before, value, after], axis=1)


def group_sum(value):
    devices = lax.axis_size("row")
    step = 1
    while step < devices:
        pairs = [(i, i ^ step) for i in range(devices)]
        value = value + lax.ppermute(value, "row", pairs)
        step *= 2
    return value


def gather_stages(value, axis, radices):
    devices = lax.axis_size(axis)
    at = lax.axis_index(axis)
    places = []
    place = 1
    for radix in radices:
        places.append(place)
        place *= radix
    for stage, (radix, place) in enumerate(reversed(list(zip(radices, places)))):
        digit = (at // place) % radix
        got = [value]
        for shift in range(1, radix):
            pairs = []
            for src in range(devices):
                d = (src // place) % radix
                pairs.append((src, src + ((d + shift) % radix - d) * place))
            got.append(lax.ppermute(value, axis, pairs))
        if radix == 2:
            first = digit == 0
            value = jnp.stack(
                [jnp.where(first, got[0], got[1]), jnp.where(first, got[1], got[0])], axis=stage
            )
        else:
            stacked = jnp.stack(got, axis=stage)
            order = (digit - jnp.arange(radix)) % radix
            value = jnp.take(stacked, order, axis=stage)
    return value.reshape((devices,) + value.shape[len(radices) :])


def radix_split(count):
    parts = []
    for radix in (3, 2):
        while count % radix == 0 and count > 1:
            parts.append(radix)
            count //= radix
    assert count == 1
    return parts


def cell_norm(values, gain):
    center = values - jnp.mean(values, axis=-1, keepdims=True)
    spread = jnp.mean(center * center, axis=-1, keepdims=True)
    return center * lax.rsqrt(spread + 1e-06) * gain


def unit_rows(values):
    return values * lax.rsqrt(jnp.sum(values * values, axis=-1, keepdims=True) + 1e-06)


def depthwise_rows(field, kernel, beside=None):
    batch_rows, row_count, width, channels = field.shape
    framed = halo_rows(field, 3)
    framed, beside = lax.optimization_barrier((framed, beside))
    framed = jnp.pad(framed, ((0, 0), (0, 0), (3, 3), (0, 0)))
    summed = jnp.zeros(field.shape, jnp.float32)
    for tap_row in range(7):
        for tap_col in range(7):
            window = framed[:, tap_row : tap_row + row_count, tap_col : tap_col + width, :].astype(
                jnp.float32
            )
            summed = summed + window * kernel[tap_row, tap_col].astype(jnp.float32)
    return summed, beside


def local(
    section_map,
    dw_kernel,
    conv_bias,
    ln_gain,
    layer_scale,
    head_gain,
    head_weight,
    texts,
    positives,
    sources,
    numerators,
):
    batch_rows, row_count, width, channels = section_map.shape
    img_count = lax.axis_size("img")
    dp_count = lax.axis_size("dp")
    dp_at = lax.axis_index("dp")
    img_at = lax.axis_index("img")
    text_f = texts.astype(jnp.float32)
    text_vec = unit_rows(text_f).astype(jnp.bfloat16)
    text_count = texts.shape[0]
    share = text_count // img_count
    text_share = lax.dynamic_slice_in_dim(text_vec, img_at * share, share)
    count = dp_count * text_count

    def in_gathered_order(vector):
        return jnp.transpose(vector.reshape(dp_count, batch_rows, img_count), (0, 2, 1)).reshape(-1)

    positives_g = in_gathered_order(positives)
    sources_g = in_gathered_order(sources)
    labels = jnp.where(positives_g[:, None] == jnp.arange(count)[None, :], 1.0, -1.0).astype(
        jnp.float32
    )
    source_table = (sources_g[:, None] == jnp.arange(SOURCES)[None, :]).astype(jnp.float32)
    weights = (
        SOURCES
        * jnp.sum(source_table * numerators.astype(jnp.float32)[None, :], axis=1)
        / jnp.sum(numerators).astype(jnp.float32)
    )
    early = (text_share, labels, source_table, weights)
    conved, early = depthwise_rows(section_map, dw_kernel, early)
    text_share, labels, source_table, weights = early
    conved = conved + conv_bias
    section_out = section_map.astype(jnp.float32) + layer_scale * cell_norm(conved, ln_gain)
    partial_value = jnp.sum(section_out, axis=(1, 2)) / (H * W)
    pooled = group_sum(partial_value)
    head_in = cell_norm(pooled, head_gain).astype(jnp.bfloat16)
    embed = jnp.dot(head_in, head_weight, preferred_element_type=jnp.float32)
    image_vec = unit_rows(embed).astype(jnp.bfloat16)
    payload = jnp.concatenate([image_vec, text_share], axis=0)
    gathered = gather_stages(payload, "img", radix_split(img_count))
    gathered = gather_stages(gathered, "dp", radix_split(dp_count))
    image_all = gathered[:, :, :batch_rows, :].reshape(dp_count * img_count * batch_rows, -1)
    text_all = gathered[:, :, batch_rows:, :].reshape(dp_count * text_count, -1)
    own_at = (dp_at * img_count + img_at) * batch_rows
    own_labels = lax.dynamic_slice_in_dim(labels, own_at, batch_rows, axis=0)
    own_weights = lax.dynamic_slice_in_dim(weights, own_at, batch_rows)
    own_logits = (
        LOGIT_SCALE * jnp.dot(image_vec, text_all.T, preferred_element_type=jnp.float32)
        + LOGIT_BIAS
    )
    own_pair = (
        own_weights[:, None] * -own_labels * jax.nn.sigmoid(-own_labels * own_logits)
    ).astype(jnp.bfloat16)
    image_dir = LOGIT_SCALE * jnp.dot(own_pair, text_all, preferred_element_type=jnp.float32)
    embed_back = jax.vjp(unit_rows, embed)[1]
    embed_grad = embed_back(image_dir)[0].astype(jnp.bfloat16)
    head_grad = jnp.dot(embed_grad, head_weight.T, preferred_element_type=jnp.float32)
    pool_back = jax.vjp(lambda values: cell_norm(values, head_gain), pooled)[1]
    own_grad = pool_back(head_grad)[0]
    norm_back = jax.vjp(lambda values: cell_norm(values, ln_gain), conved)[1]
    seeded = jnp.broadcast_to((layer_scale * own_grad)[:, None, None, :], conved.shape)
    conv_grad = norm_back(seeded)[0].astype(jnp.bfloat16)
    image_all, conv_grad = lax.optimization_barrier((image_all, conv_grad))
    logits = (
        LOGIT_SCALE * jnp.dot(image_all, text_all.T, preferred_element_type=jnp.float32)
        + LOGIT_BIAS
    )
    pair_grad = (weights[:, None] * -labels * jax.nn.sigmoid(-labels * logits)).astype(
        jnp.bfloat16
    )
    row_loss = lax.optimization_barrier(jnp.sum(jax.nn.softplus(-labels * logits), axis=1))
    group_sums = jnp.sum(source_table * (weights * row_loss)[:, None], axis=0)
    text_pair = lax.dynamic_slice_in_dim(pair_grad, dp_at * text_count, text_count, axis=1)
    text_dir = LOGIT_SCALE * lax.dot_general(
        text_pair, image_all, (((0,), (0,)), ((), ())), preferred_element_type=jnp.float32
    )
    text_back = jax.vjp(unit_rows, text_f)[1]
    text_grad = text_back(text_dir)[0]
    spread = depthwise_rows(conv_grad, dw_kernel[::-1, ::-1, :])[0]
    grad_map = (own_grad[:, None, None, :] + spread).astype(jnp.bfloat16)
    return (grad_map, text_grad, group_sums)


def solution(mesh):
    dp_count, tile_count = mesh.devices.shape

    def run(section_map, *rest):
        rows_each = section_map.shape[1] // tile_count
        per_image = H // rows_each
        assert per_image & (per_image - 1) == 0
        split = Mesh(
            mesh.devices.reshape(dp_count, tile_count // per_image, per_image),
            ("dp", "img", "row"),
        )
        tiled = ("img", "row")
        placed = (
            P("dp", tiled, None, None),
            P(),
            P(),
            P(),
            P(),
            P(),
            P(),
            P("dp", None),
            P(),
            P(),
            P(),
        )
        return jax.shard_map(
            local,
            mesh=split,
            in_specs=placed,
            out_specs=(P("dp", tiled, None, None), P("dp", None), P()),
            check_vma=False,
        )(section_map, *rest)

    return run
```

```python
import jax
import jax.numpy as jnp
from jax import lax
from jax.sharding import Mesh
from jax.sharding import PartitionSpec as P

H = 32
W = 32
SOURCES = 32


LOGIT_SCALE = 10.0
LOGIT_BIAS = -5.0


def halo_rows(value, width):
    devices = lax.axis_size("row")
    up = [(i, i + 1) for i in range(devices - 1)]
    down = [(j, i) for i, j in up]
    length = value.shape[1]
    last = lax.slice_in_dim(value, length - width, length, axis=1)
    leading = lax.slice_in_dim(value, 0, width, axis=1)
    before = lax.ppermute(last, "row", up)
    after = lax.ppermute(leading, "row", down)
    return jnp.concatenate([before, value, after], axis=1)


def group_sum(value):
    devices = lax.axis_size("row")
    step = 1
    while step < devices:
        pairs = [(i, i ^ step) for i in range(devices)]
        value = value + lax.ppermute(value, "row", pairs)
        step *= 2
    return value


def gather_stages(value, axis, radices):
    devices = lax.axis_size(axis)
    at = lax.axis_index(axis)
    places = []
    place = 1
    for radix in radices:
        places.append(place)
        place *= radix
    for stage, (radix, place) in enumerate(reversed(list(zip(radices, places)))):
        digit = (at // place) % radix
        got = [value]
        for shift in range(1, radix):
            pairs = []
            for src in range(devices):
                d = (src // place) % radix
                pairs.append((src, src + ((d + shift) % radix - d) * place))
            got.append(lax.ppermute(value, axis, pairs))
        if radix == 2:
            first = digit == 0
            value = jnp.stack(
                [jnp.where(first, got[0], got[1]), jnp.where(first, got[1], got[0])], axis=stage
            )
        else:
            stacked = jnp.stack(got, axis=stage)
            order = (digit - jnp.arange(radix)) % radix
            value = jnp.take(stacked, order, axis=stage)
    return value.reshape((devices,) + value.shape[len(radices) :])


def radix_split(count):
    parts = []
    for radix in (4, 3, 2):
        while count % radix == 0 and count > 1:
            parts.append(radix)
            count //= radix
    assert count == 1
    return parts


def cell_norm(values, gain):
    center = values - jnp.mean(values, axis=-1, keepdims=True)
    spread = jnp.mean(center * center, axis=-1, keepdims=True)
    return center * lax.rsqrt(spread + 1e-06) * gain


def unit_rows(values):
    return values * lax.rsqrt(jnp.sum(values * values, axis=-1, keepdims=True) + 1e-06)


def depthwise_rows(field, kernel, beside=None):
    batch_rows, row_count, width, channels = field.shape
    framed = halo_rows(field, 3)
    framed, beside = lax.optimization_barrier((framed, beside))
    framed = jnp.pad(framed, ((0, 0), (0, 0), (3, 3), (0, 0)))
    summed = jnp.zeros(field.shape, jnp.float32)
    for tap_row in range(7):
        for tap_col in range(7):
            window = framed[:, tap_row : tap_row + row_count, tap_col : tap_col + width, :].astype(
                jnp.float32
            )
            summed = summed + window * kernel[tap_row, tap_col].astype(jnp.float32)
    return summed, beside


def local(
    section_map,
    dw_kernel,
    conv_bias,
    ln_gain,
    layer_scale,
    head_gain,
    head_weight,
    texts,
    positives,
    sources,
    numerators,
):
    batch_rows, row_count, width, channels = section_map.shape
    img_count = lax.axis_size("img")
    dp_count = lax.axis_size("dp")
    dp_at = lax.axis_index("dp")
    img_at = lax.axis_index("img")
    text_f = texts.astype(jnp.float32)
    text_vec = unit_rows(text_f).astype(jnp.bfloat16)
    text_count = texts.shape[0]
    share = text_count // img_count
    text_share = lax.dynamic_slice_in_dim(text_vec, img_at * share, share)
    count = dp_count * text_count

    def in_gathered_order(vector):
        return jnp.transpose(vector.reshape(dp_count, batch_rows, img_count), (0, 2, 1)).reshape(-1)

    positives_g = in_gathered_order(positives)
    sources_g = in_gathered_order(sources)
    labels = jnp.where(positives_g[:, None] == jnp.arange(count)[None, :], 1.0, -1.0).astype(
        jnp.float32
    )
    source_table = (sources_g[:, None] == jnp.arange(SOURCES)[None, :]).astype(jnp.float32)
    weights = (
        SOURCES
        * jnp.sum(source_table * numerators.astype(jnp.float32)[None, :], axis=1)
        / jnp.sum(numerators).astype(jnp.float32)
    )
    early = (text_share, labels, source_table, weights)
    conved, early = depthwise_rows(section_map, dw_kernel, early)
    text_share, labels, source_table, weights = early
    conved = conved + conv_bias
    section_out = section_map.astype(jnp.float32) + layer_scale * cell_norm(conved, ln_gain)
    partial_value = jnp.sum(section_out, axis=(1, 2)) / (H * W)
    pooled = group_sum(partial_value)
    head_in = cell_norm(pooled, head_gain).astype(jnp.bfloat16)
    embed = jnp.dot(head_in, head_weight, preferred_element_type=jnp.float32)
    image_vec = unit_rows(embed).astype(jnp.bfloat16)
    payload = jnp.concatenate([image_vec, text_share], axis=0)
    gathered = gather_stages(payload, "img", radix_split(img_count))
    gathered = gather_stages(gathered, "dp", radix_split(dp_count))
    image_all = gathered[:, :, :batch_rows, :].reshape(dp_count * img_count * batch_rows, -1)
    text_all = gathered[:, :, batch_rows:, :].reshape(dp_count * text_count, -1)
    logits = (
        LOGIT_SCALE * jnp.dot(image_all, text_all.T, preferred_element_type=jnp.float32)
        + LOGIT_BIAS
    )
    pair_grad = (weights[:, None] * -labels * jax.nn.sigmoid(-labels * logits)).astype(
        jnp.bfloat16
    )
    own_at = (dp_at * img_count + img_at) * batch_rows
    own_pair = lax.dynamic_slice_in_dim(pair_grad, own_at, batch_rows, axis=0)
    image_dir = LOGIT_SCALE * jnp.dot(own_pair, text_all, preferred_element_type=jnp.float32)
    embed_back = jax.vjp(unit_rows, embed)[1]
    embed_grad = embed_back(image_dir)[0].astype(jnp.bfloat16)
    head_grad = jnp.dot(embed_grad, head_weight.T, preferred_element_type=jnp.float32)
    pool_back = jax.vjp(lambda values: cell_norm(values, head_gain), pooled)[1]
    own_grad = pool_back(head_grad)[0]
    norm_back = jax.vjp(lambda values: cell_norm(values, ln_gain), conved)[1]
    seeded = jnp.broadcast_to((layer_scale * own_grad)[:, None, None, :], conved.shape)
    conv_grad = norm_back(seeded)[0].astype(jnp.bfloat16)
    logits, pair_grad, conv_grad = lax.optimization_barrier((logits, pair_grad, conv_grad))
    row_loss = lax.optimization_barrier(jnp.sum(jax.nn.softplus(-labels * logits), axis=1))
    group_sums = jnp.sum(source_table * (weights * row_loss)[:, None], axis=0)
    text_pair = lax.dynamic_slice_in_dim(pair_grad, dp_at * text_count, text_count, axis=1)
    text_dir = LOGIT_SCALE * lax.dot_general(
        text_pair, image_all, (((0,), (0,)), ((), ())), preferred_element_type=jnp.float32
    )
    text_back = jax.vjp(unit_rows, text_f)[1]
    text_grad = text_back(text_dir)[0]
    spread = depthwise_rows(conv_grad, dw_kernel[::-1, ::-1, :])[0]
    grad_map = (own_grad[:, None, None, :] + spread).astype(jnp.bfloat16)
    return (grad_map, text_grad, group_sums)


def solution(mesh):
    dp_count, tile_count = mesh.devices.shape

    def run(section_map, *rest):
        rows_each = section_map.shape[1] // tile_count
        per_image = H // rows_each
        assert per_image & (per_image - 1) == 0
        split = Mesh(
            mesh.devices.reshape(dp_count, tile_count // per_image, per_image),
            ("dp", "img", "row"),
        )
        tiled = ("img", "row")
        placed = (
            P("dp", tiled, None, None),
            P(),
            P(),
            P(),
            P(),
            P(),
            P(),
            P("dp", None),
            P(),
            P(),
            P(),
        )
        return jax.shard_map(
            local,
            mesh=split,
            in_specs=placed,
            out_specs=(P("dp", tiled, None, None), P("dp", None), P()),
            check_vma=False,
        )(section_map, *rest)

    return run
```
